512 devices in a mesh: pts: 32 (over z_hi, y, core), lists: 16 (over x, z_lo).
Axes of the slice: x: 4, y: 4, z: 16 (z_hi: 4, z_lo: 4; z = z_hi * 4 + z_lo), core: 2. Of those that a mesh axis runs over, the one named last changes fastest.
Arguments:
- points: bfloat16 [12288, 256], P('pts'), may hold values from -4 to 4
- centroids: bfloat16 [65536, 256], P('lists'), may hold values from -0.375 to 0.375
- prior: int32 [12288], P('pts'), may hold values from 0 to 65535
- loads: int32 [65536], P('lists'), may hold values from 2 to 14, as said below
Outputs:
- centroid_means: float32 [256, 65536], P('pts', 'lists')
- log_col_scale: float32 [65536], P('lists')
The draws below stay inside these ranges and needn't reach their ends.
Inputs may be any that keep to these rules, and one draw needn't show every extreme that they name: Lists 2k and 2k + 1 have loads 8 + e and 8 - e for some e of 0 to 6, so all loads sum to 524288.
All inputs are finite; a program needn't handle non-finite values.
Results may differ from the reference program's by a relative error of at most 0.003.
Values sent between devices are 32-bit elements; how exact they have to be, the bound alone decides.
No kernel may reach another device: no remote copies, remote signals or barrier semaphores. Data moves between devices by JAX's collectives and lax.ppermute only.
A program may use at most 64 MiB of HBM per device.

```python
import jax
import jax.numpy as jnp
from jax import lax

DIM = 256
ITERS = 3
BLOCK = 512
LISTS = 65536
NPTS = 12288


def draw_loads(key, part):
    spread = jax.random.randint(key, (LISTS // 2,), 0, 7).astype(jnp.int32)
    return jnp.stack([8 + spread, 8 - spread], axis=1).reshape(LISTS).astype(jnp.int32)


def place_ends(result, rng, smallest, largest):
    extent = result.shape
    index_at = [jax.random.randint(jax.random.fold_in(rng, axis), (), 0, extent[axis]) for axis in range(len(extent))]
    result = result.at[tuple(index_at)].set(smallest)
    longest = extent.index(max(extent))
    index_at[longest] = (index_at[longest] + 1) % extent[longest]
    return result.at[tuple(index_at)].set(largest)


def shard_levels(key, shape, split, least, high):
    factor_of, own = 1.0, jax.random.fold_in(key, 6)
    for axis_at, shards_of in split:
        draws = jnp.exp(jax.random.uniform(jax.random.fold_in(own, axis_at), (shards_of,), jnp.float32, least / len(split), high / len(split)))
        factor_of = factor_of * jnp.repeat(draws, shape[axis_at] // shards_of).reshape([-1 if axis == axis_at else 1 for axis in range(len(shape))])
    return factor_of


def centred(stream_key, shape, deviation, reach, shards=(), dtype=jnp.bfloat16):
    level = shard_levels(stream_key, shape, shards, -0.22, 0.18) if shards else 1.0
    array = jax.random.normal(stream_key, shape, jnp.float32) * deviation * level
    return jnp.minimum(jnp.maximum(array, -reach), reach).astype(dtype)


def setup_inputs(seed: int = 0) -> dict:
    streams_of = jax.random.split(jax.random.key(seed), 5)
    return {
        "points": centred(streams_of[0], (NPTS, DIM), 1.0, 4.0, ((0, 32),)),
        "centroids": centred(streams_of[1], (LISTS, DIM), DIM ** -0.5, 0.375, ((0, 16),)),
        "prior": place_ends(jax.random.randint(streams_of[2], (NPTS,), 0, LISTS), jax.random.fold_in(streams_of[2], 1), 0, LISTS - 1).astype(jnp.int32),
        "loads": draw_loads(jax.random.fold_in(streams_of[4], 71), 0),
    }


def kernel_tile(points, cent_block, prior, start):
    score = lax.dot_general(points, cent_block, (((1,), (1,)), ((), ())), preferred_element_type=jnp.float32)
    cols = start + lax.iota(jnp.int32, cent_block.shape[0])
    hit = (prior[:, None] == cols[None, :]).astype(jnp.float32)
    return jnp.exp(3.0 * score + 10.0 * hit)


def reference(points, centroids, prior, loads):
    count = LISTS // BLOCK
    target = loads.astype(jnp.float32) * (NPTS / (8.0 * LISTS))
    starts = (jnp.arange(count) * BLOCK).astype(jnp.int32)

    def tile(start):
        block = lax.dynamic_slice_in_dim(centroids, start, BLOCK, 0)
        return kernel_tile(points, block, prior, start)

    col_scale = jnp.ones((LISTS,), jnp.float32)
    row_scale = jnp.ones((NPTS,), jnp.float32)
    for step in range(ITERS):
        def add_rows(carry, start):
            part = lax.dynamic_slice_in_dim(col_scale, start, BLOCK, 0)
            return carry + jnp.sum(tile(start) * part[None, :], axis=1), None

        row_total, _ = lax.scan(add_rows, jnp.zeros((NPTS,), jnp.float32), starts)
        row_scale = 1.0 / row_total
        col_total = lax.map(lambda start: jnp.sum(tile(start) * row_scale[:, None], axis=0), starts).reshape(LISTS)
        col_scale = target / col_total

    def sums_of(start):
        part = lax.dynamic_slice_in_dim(col_scale, start, BLOCK, 0)
        plan = (tile(start) * row_scale[:, None] * part[None, :]).astype(jnp.bfloat16)
        return lax.dot_general(points, plan, (((0,), (0,)), ((), ())), preferred_element_type=jnp.float32)

    sums = lax.map(sums_of, starts)
    sums = jnp.transpose(sums, (1, 0, 2)).reshape(DIM, LISTS)
    return sums / target[None, :], jnp.log(col_scale)
```

```python
import jax
import jax.numpy as jnp
from jax import lax
from jax.sharding import Mesh, PartitionSpec as P

ITERS = 3
BLOCK = 512


def kernel_tile(points, cent_block, prior, start):
    score = lax.dot_general(
        points, cent_block, (((1,), (1,)), ((), ())), preferred_element_type=jnp.float32
    )
    cols = start + lax.iota(jnp.int32, cent_block.shape[0])
    hit = (prior[:, None] == cols[None, :]).astype(jnp.float32)
    return jnp.exp(3.0 * score + 10.0 * hit)


PTS_AXES = (("z_hi", 4), ("y", 4), ("core", 2))
LISTS_AXES = (("x", 4), ("z_lo", 4))
PTS = tuple(name for name, _ in PTS_AXES)
LISTS = tuple(name for name, _ in LISTS_AXES)


def point_mass(partial_value):
    return lax.psum(lax.psum(partial_value, "z_lo"), "x")


def list_mass(partial_value):
    return lax.psum(lax.psum(lax.psum(partial_value, "core"), "y"), "z_hi")


def scatter_rows(points):
    n = points.shape[0]
    sizes = [size for _, size in PTS_AXES]
    rows = points.shape[1] // (sizes[0] * sizes[1] * sizes[2])
    blocked = points.reshape(n, sizes[0], sizes[1], sizes[2], rows)
    return blocked.transpose(0, 3, 2, 1, 4).reshape(n, points.shape[1])


def sum_scatter(value):
    for name in ("core", "y", "z_hi"):
        value = lax.psum_scatter(value, name, scatter_dimension=0, tiled=True)
    return value


def local(points, centroids, prior, loads):
    n_lists = centroids.shape[0]
    count = n_lists // BLOCK
    offset = (lax.axis_index("x") * lax.axis_size("z_lo") + lax.axis_index("z_lo")) * n_lists
    total_pts = points.shape[0] * lax.axis_size(PTS)
    total_lists = n_lists * lax.axis_size(LISTS)
    target = loads.astype(jnp.float32) * (total_pts / (8.0 * total_lists))

    def tile(index):
        block = centroids[index * BLOCK : (index + 1) * BLOCK]
        return kernel_tile(points, block, prior, offset + index * BLOCK)

    col_scale = jnp.ones((n_lists,), jnp.float32)
    row_scale = jnp.ones((points.shape[0],), jnp.float32)
    for step in range(ITERS):
        partial_value = jnp.zeros((points.shape[0],), jnp.float32)
        for index in range(count):
            partial_value = partial_value + jnp.sum(
                tile(index) * col_scale[None, index * BLOCK : (index + 1) * BLOCK], axis=1
            )
        row_scale = 1.0 / point_mass(partial_value)
        pieces = [jnp.sum(tile(index) * row_scale[:, None], axis=0) for index in range(count)]
        col_scale = target / list_mass(jnp.concatenate(pieces))
    plan = jnp.concatenate(
        [
            (
                tile(index)
                * row_scale[:, None]
                * col_scale[None, index * BLOCK : (index + 1) * BLOCK]
            ).astype(jnp.bfloat16)
            for index in range(count)
        ],
        axis=1,
    )
    sums = sum_scatter(
        lax.dot_general(scatter_rows(points), plan, (((0,), (0,)), ((), ())), preferred_element_type=jnp.float32)
    )
    return (sums / target[None, :], jnp.log(col_scale))


def solution(mesh):
    sizes = [size for _, size in PTS_AXES + LISTS_AXES]
    assert mesh.shape["pts"] == sizes[0] * sizes[1] * sizes[2]
    assert mesh.shape["lists"] == sizes[3] * sizes[4]
    fine = Mesh(mesh.devices.reshape(sizes), PTS + LISTS)
    return jax.shard_map(
        local,
        mesh=fine,
        in_specs=(P(PTS, None), P(LISTS, None), P(PTS), P(LISTS)),
        out_specs=(P(PTS, LISTS), P(LISTS)),
        check_vma=False,
    )
```

```python
import jax
import jax.numpy as jnp
from jax import lax
from jax.sharding import Mesh, PartitionSpec as P

ITERS = 3
BLOCK = 512


def kernel_tile(points, cent_block, prior, start):
    score = lax.dot_general(
        points, cent_block, (((1,), (1,)), ((), ())), preferred_element_type=jnp.float32
    )
    cols = start + lax.iota(jnp.int32, cent_block.shape[0])
    hit = (prior[:, None] == cols[None, :]).astype(jnp.float32)
    return jnp.exp(3.0 * score + 10.0 * hit)


PTS_AXES = (("z_hi", 4), ("y", 4), ("core", 2))
LISTS_AXES = (("x", 4), ("z_lo", 4))
PTS = tuple(name for name, _ in PTS_AXES)
LISTS = tuple(name for name, _ in LISTS_AXES)


def point_mass(partial_value):
    return lax.psum(lax.psum(partial_value, "z_lo"), "x")


def list_mass(partial_value):
    return lax.psum(lax.psum(lax.psum(partial_value, "core"), "y"), "z_hi")


def scatter_rows(points):
    n = points.shape[0]
    sizes = [size for _, size in PTS_AXES]
    rows = points.shape[1] // (sizes[0] * sizes[1] * sizes[2])
    blocked = points.reshape(n, sizes[0], sizes[1], sizes[2], rows)
    return blocked.transpose(0, 3, 2, 1, 4).reshape(n, points.shape[1])


def sum_scatter(value):
    for name in ("core", "y", "z_hi"):
        n = lax.axis_size(name)
        blocks = value.reshape(n, value.shape[0] // n, value.shape[1])
        value = jnp.sum(lax.all_to_all(blocks, name, 0, 0), axis=0)
    return value


def local(points, centroids, prior, loads):
    n_lists = centroids.shape[0]
    count = n_lists // BLOCK
    offset = (lax.axis_index("x") * lax.axis_size("z_lo") + lax.axis_index("z_lo")) * n_lists
    total_pts = points.shape[0] * lax.axis_size(PTS)
    total_lists = n_lists * lax.axis_size(LISTS)
    target = loads.astype(jnp.float32) * (total_pts / (8.0 * total_lists))

    def tile(index):
        block = centroids[index * BLOCK : (index + 1) * BLOCK]
        return kernel_tile(points, block, prior, offset + index * BLOCK)

    col_scale = jnp.ones((n_lists,), jnp.float32)
    row_scale = jnp.ones((points.shape[0],), jnp.float32)
    for step in range(ITERS):
        partial_value = jnp.zeros((points.shape[0],), jnp.float32)
        for index in range(count):
            partial_value = partial_value + jnp.sum(
                tile(index) * col_scale[None, index * BLOCK : (index + 1) * BLOCK], axis=1
            )
        row_scale = 1.0 / point_mass(partial_value)
        pieces = [jnp.sum(tile(index) * row_scale[:, None], axis=0) for index in range(count)]
        col_scale = target / list_mass(jnp.concatenate(pieces))
    plan = jnp.concatenate(
        [
            (
                tile(index)
                * row_scale[:, None]
                * col_scale[None, index * BLOCK : (index + 1) * BLOCK]
            ).astype(jnp.bfloat16)
            for index in range(count)
        ],
        axis=1,
    )
    sums = sum_scatter(
        lax.dot_general(scatter_rows(points), plan, (((0,), (0,)), ((), ())), preferred_element_type=jnp.float32)
    )
    return (sums / target[None, :], jnp.log(col_scale))


def solution(mesh):
    sizes = [size for _, size in PTS_AXES + LISTS_AXES]
    assert mesh.shape["pts"] == sizes[0] * sizes[1] * sizes[2]
    assert mesh.shape["lists"] == sizes[3] * sizes[4]
    fine = Mesh(mesh.devices.reshape(sizes), PTS + LISTS)
    return jax.shard_map(
        local,
        mesh=fine,
        in_specs=(P(PTS, None), P(LISTS, None), P(PTS), P(LISTS)),
        out_specs=(P(PTS, LISTS), P(LISTS)),
        check_vma=False,
    )
```

```python
import jax
import jax.numpy as jnp
from jax import lax
from jax.sharding import Mesh, PartitionSpec as P

ITERS = 3
BLOCK = 512


def kernel_tile(points, cent_block, prior, start):
    score = lax.dot_general(
        points, cent_block, (((1,), (1,)), ((), ())), preferred_element_type=jnp.float32
    )
    cols = start + lax.iota(jnp.int32, cent_block.shape[0])
    hit = (prior[:, None] == cols[None, :]).astype(jnp.float32)
    return jnp.exp(3.0 * score + 10.0 * hit)


PTS_AXES = (("z_hi", 4), ("y", 4), ("core", 2))
LISTS_AXES = (("x", 4), ("z_lo", 4))
PTS = tuple(name for name, _ in PTS_AXES)
LISTS = tuple(name for name, _ in LISTS_AXES)


def exchange_sum(value, names):
    n = lax.axis_size(names)
    copies = jnp.broadcast_to(value[None], (n,) + value.shape)
    return jnp.sum(lax.all_to_all(copies, names, 0, 0), axis=0)


def point_mass(partial_value):
    return exchange_sum(partial_value, LISTS)


def list_mass(partial_value):
    for name in ("core", "y", "z_hi"):
        partial_value = exchange_sum(partial_value, name)
    return partial_value


def scatter_rows(points):
    n = points.shape[0]
    sizes = [size for _, size in PTS_AXES]
    rows = points.shape[1] // (sizes[0] * sizes[1] * sizes[2])
    blocked = points.reshape(n, sizes[0], sizes[1], sizes[2], rows)
    return blocked.transpose(0, 3, 2, 1, 4).reshape(n, points.shape[1])


def sum_scatter(value):
    for name in ("core", "y", "z_hi"):
        n = lax.axis_size(name)
        blocks = value.reshape(n, value.shape[0] // n, value.shape[1])
        value = jnp.sum(lax.all_to_all(blocks, name, 0, 0), axis=0)
    return value


def local(points, centroids, prior, loads):
    n_lists = centroids.shape[0]
    count = n_lists // BLOCK
    offset = (lax.axis_index("x") * lax.axis_size("z_lo") + lax.axis_index("z_lo")) * n_lists
    total_pts = points.shape[0] * lax.axis_size(PTS)
    total_lists = n_lists * lax.axis_size(LISTS)
    target = loads.astype(jnp.float32) * (total_pts / (8.0 * total_lists))

    def tile(index):
        block = centroids[index * BLOCK : (index + 1) * BLOCK]
        return kernel_tile(points, block, prior, offset + index * BLOCK)

    col_scale = jnp.ones((n_lists,), jnp.float32)
    row_scale = jnp.ones((points.shape[0],), jnp.float32)
    for step in range(ITERS):
        partial_value = jnp.zeros((points.shape[0],), jnp.float32)
        for index in range(count):
            partial_value = partial_value + jnp.sum(
                tile(index) * col_scale[None, index * BLOCK : (index + 1) * BLOCK], axis=1
            )
        row_scale = 1.0 / point_mass(partial_value)
        pieces = [jnp.sum(tile(index) * row_scale[:, None], axis=0) for index in range(count)]
        col_scale = target / list_mass(jnp.concatenate(pieces))
    plan = jnp.concatenate(
        [
            (
                tile(index)
                * row_scale[:, None]
                * col_scale[None, index * BLOCK : (index + 1) * BLOCK]
            ).astype(jnp.bfloat16)
            for index in range(count)
        ],
        axis=1,
    )
    sums = sum_scatter(
        lax.dot_general(scatter_rows(points), plan, (((0,), (0,)), ((), ())), preferred_element_type=jnp.float32)
    )
    return (sums / target[None, :], jnp.log(col_scale))


def solution(mesh):
    sizes = [size for _, size in PTS_AXES + LISTS_AXES]
    assert mesh.shape["pts"] == sizes[0] * sizes[1] * sizes[2]
    assert mesh.shape["lists"] == sizes[3] * sizes[4]
    fine = Mesh(mesh.devices.reshape(sizes), PTS + LISTS)
    return jax.shard_map(
        local,
        mesh=fine,
        in_specs=(P(PTS, None), P(LISTS, None), P(PTS), P(LISTS)),
        out_specs=(P(PTS, LISTS), P(LISTS)),
        check_vma=False,
    )
```

```python
import jax
import jax.numpy as jnp
from jax import lax
from jax.sharding import Mesh, PartitionSpec as P

ITERS = 3
BLOCK = 512


def kernel_tile(points, cent_block, prior, start):
    score = lax.dot_general(
        points, cent_block, (((1,), (1,)), ((), ())), preferred_element_type=jnp.float32
    )
    cols = start + lax.iota(jnp.int32, cent_block.shape[0])
    hit = (prior[:, None] == cols[None, :]).astype(jnp.float32)
    return jnp.exp(3.0 * score + 10.0 * hit)


PTS_AXES = (("z_hi", 4), ("y", 4), ("core", 2))
LISTS_AXES = (("x", 4), ("z_lo", 4))
PTS = tuple(name for name, _ in PTS_AXES)
LISTS = tuple(name for name, _ in LISTS_AXES)


def exchange_sum(value, names):
    n = lax.axis_size(names)
    copies = jnp.broadcast_to(value[None], (n,) + value.shape)
    return jnp.sum(lax.all_to_all(copies, names, 0, 0), axis=0)


def point_mass(partial_value):
    return exchange_sum(partial_value, LISTS)


def list_mass(partial_value):
    return exchange_sum(exchange_sum(partial_value, ("y", "core")), "z_hi")


def scatter_rows(points):
    n = points.shape[0]
    sizes = [size for _, size in PTS_AXES]
    rows = points.shape[1] // (sizes[0] * sizes[1] * sizes[2])
    blocked = points.reshape(n, sizes[0], sizes[1], sizes[2], rows)
    return blocked.transpose(0, 3, 2, 1, 4).reshape(n, points.shape[1])


def sum_scatter(value):
    for name in ("core", "y", "z_hi"):
        n = lax.axis_size(name)
        blocks = value.reshape(n, value.shape[0] // n, value.shape[1])
        value = jnp.sum(lax.all_to_all(blocks, name, 0, 0), axis=0)
    return value


def local(points, centroids, prior, loads):
    n_lists = centroids.shape[0]
    count = n_lists // BLOCK
    offset = (lax.axis_index("x") * lax.axis_size("z_lo") + lax.axis_index("z_lo")) * n_lists
    total_pts = points.shape[0] * lax.axis_size(PTS)
    total_lists = n_lists * lax.axis_size(LISTS)
    target = loads.astype(jnp.float32) * (total_pts / (8.0 * total_lists))

    def tile(index):
        block = centroids[index * BLOCK : (index + 1) * BLOCK]
        return kernel_tile(points, block, prior, offset + index * BLOCK)

    col_scale = jnp.ones((n_lists,), jnp.float32)
    row_scale = jnp.ones((points.shape[0],), jnp.float32)
    for step in range(ITERS):
        partial_value = jnp.zeros((points.shape[0],), jnp.float32)
        for index in range(count):
            partial_value = partial_value + jnp.sum(
                tile(index) * col_scale[None, index * BLOCK : (index + 1) * BLOCK], axis=1
            )
        row_scale = 1.0 / point_mass(partial_value)
        pieces = [jnp.sum(tile(index) * row_scale[:, None], axis=0) for index in range(count)]
        col_scale = target / list_mass(jnp.concatenate(pieces))
    plan = jnp.concatenate(
        [
            (
                tile(index)
                * row_scale[:, None]
                * col_scale[None, index * BLOCK : (index + 1) * BLOCK]
            ).astype(jnp.bfloat16)
            for index in range(count)
        ],
        axis=1,
    )
    sums = sum_scatter(
        lax.dot_general(scatter_rows(points), plan, (((0,), (0,)), ((), ())), preferred_element_type=jnp.float32)
    )
    return (sums / target[None, :], jnp.log(col_scale))


def solution(mesh):
    sizes = [size for _, size in PTS_AXES + LISTS_AXES]
    assert mesh.shape["pts"] == sizes[0] * sizes[1] * sizes[2]
    assert mesh.shape["lists"] == sizes[3] * sizes[4]
    fine = Mesh(mesh.devices.reshape(sizes), PTS + LISTS)
    return jax.shard_map(
        local,
        mesh=fine,
        in_specs=(P(PTS, None), P(LISTS, None), P(PTS), P(LISTS)),
        out_specs=(P(PTS, LISTS), P(LISTS)),
        check_vma=False,
    )
```

```python
import jax
import jax.numpy as jnp
from jax import lax
from jax.sharding import Mesh, PartitionSpec as P

ITERS = 3


def kernel_tile(points, cent_block, prior, start):
    score = lax.dot_general(
        points, cent_block, (((1,), (1,)), ((), ())), preferred_element_type=jnp.float32
    )
    cols = start + lax.iota(jnp.int32, cent_block.shape[0])
    hit = (prior[:, None] == cols[None, :]).astype(jnp.float32)
    return jnp.exp(3.0 * score + 10.0 * hit)


PTS_AXES = (("z_hi", 4), ("y", 4), ("core", 2))
LISTS_AXES = (("x", 4), ("z_lo", 4))
PTS = tuple(name for name, _ in PTS_AXES)
LISTS = tuple(name for name, _ in LISTS_AXES)


def exchange_sum(value, names):
    n = lax.axis_size(names)
    copies = jnp.broadcast_to(value[None], (n,) + value.shape)
    return jnp.sum(lax.all_to_all(copies, names, 0, 0), axis=0)


def point_mass(partial_value):
    return exchange_sum(partial_value, LISTS)


def list_mass(partial_value):
    return exchange_sum(exchange_sum(partial_value, ("y", "core")), "z_hi")


def scatter_rows(points):
    n = points.shape[0]
    sizes = [size for _, size in PTS_AXES]
    rows = points.shape[1] // (sizes[0] * sizes[1] * sizes[2])
    blocked = points.reshape(n, sizes[0], sizes[1], sizes[2], rows)
    return blocked.transpose(0, 3, 2, 1, 4).reshape(n, points.shape[1])


def sum_scatter(value):
    for name in ("core", "y", "z_hi"):
        n = lax.axis_size(name)
        blocks = value.reshape(n, value.shape[0] // n, value.shape[1])
        value = jnp.sum(lax.all_to_all(blocks, name, 0, 0), axis=0)
    return value


def local(points, centroids, prior, loads):
    n_lists = centroids.shape[0]
    offset = (lax.axis_index("x") * lax.axis_size("z_lo") + lax.axis_index("z_lo")) * n_lists
    total_pts = points.shape[0] * lax.axis_size(PTS)
    total_lists = n_lists * lax.axis_size(LISTS)
    target = loads.astype(jnp.float32) * (total_pts / (8.0 * total_lists))

    kernel = kernel_tile(points, centroids, prior, offset)

    col_scale = jnp.ones((n_lists,), jnp.float32)
    row_scale = jnp.ones((points.shape[0],), jnp.float32)
    for step in range(ITERS):
        row_scale = 1.0 / point_mass(jnp.sum(kernel * col_scale[None, :], axis=1))
        col_scale = target / list_mass(jnp.sum(kernel * row_scale[:, None], axis=0))
    plan = (kernel * row_scale[:, None] * col_scale[None, :]).astype(jnp.bfloat16)
    sums = sum_scatter(
        lax.dot_general(scatter_rows(points), plan, (((0,), (0,)), ((), ())), preferred_element_type=jnp.float32)
    )
    return (sums / target[None, :], jnp.log(col_scale))


def solution(mesh):
    sizes = [size for _, size in PTS_AXES + LISTS_AXES]
    assert mesh.shape["pts"] == sizes[0] * sizes[1] * sizes[2]
    assert mesh.shape["lists"] == sizes[3] * sizes[4]
    fine = Mesh(mesh.devices.reshape(sizes), PTS + LISTS)
    return jax.shard_map(
        local,
        mesh=fine,
        in_specs=(P(PTS, None), P(LISTS, None), P(PTS), P(LISTS)),
        out_specs=(P(PTS, LISTS), P(LISTS)),
        check_vma=False,
    )
```

```python
import jax
import jax.numpy as jnp
from jax import lax
from jax.sharding import Mesh, PartitionSpec as P

ITERS = 3


def kernel_tile(points, cent_block, prior, start):
    score = lax.dot_general(
        points, cent_block, (((1,), (1,)), ((), ())), preferred_element_type=jnp.float32
    )
    cols = start + lax.iota(jnp.int32, cent_block.shape[0])
    hit = (prior[:, None] == cols[None, :]).astype(jnp.float32)
    return jnp.exp(3.0 * score + 10.0 * hit)


PTS_AXES = (("z_hi", 4), ("y", 4), ("core", 2))
LISTS_AXES = (("x", 4), ("z_lo", 4))
PTS = tuple(name for name, _ in PTS_AXES)
LISTS = tuple(name for name, _ in LISTS_AXES)


def exchange_sum(value, names):
    n = lax.axis_size(names)
    copies = jnp.broadcast_to(value[None], (n,) + value.shape)
    return jnp.sum(lax.all_to_all(copies, names, 0, 0), axis=0)


def point_mass(partial_value):
    return exchange_sum(partial_value, LISTS)


def list_mass(partial_value):
    return exchange_sum(exchange_sum(partial_value, ("y", "core")), "z_hi")


def scatter_rows(points):
    n = points.shape[0]
    sizes = [size for _, size in PTS_AXES]
    rows = points.shape[1] // (sizes[0] * sizes[1] * sizes[2])
    blocked = points.reshape(n, sizes[0], sizes[1], sizes[2], rows)
    return blocked.transpose(0, 3, 2, 1, 4).reshape(n, points.shape[1])


def sum_scatter(value):
    for name in ("core", "y", "z_hi"):
        n = lax.axis_size(name)
        blocks = value.reshape(n, value.shape[0] // n, value.shape[1])
        value = jnp.sum(lax.all_to_all(blocks, name, 0, 0), axis=0)
    return value


def local(points, centroids, prior, loads):
    n_lists = centroids.shape[0]
    offset = (lax.axis_index("x") * lax.axis_size("z_lo") + lax.axis_index("z_lo")) * n_lists
    total_pts = points.shape[0] * lax.axis_size(PTS)
    total_lists = n_lists * lax.axis_size(LISTS)
    target = loads.astype(jnp.float32) * (total_pts / (8.0 * total_lists))

    kernel = kernel_tile(points, centroids, prior, offset)

    col_scale = jnp.ones((n_lists,), jnp.float32)
    for step in range(ITERS - 1):
        row_scale = 1.0 / point_mass(jnp.sum(kernel * col_scale[None, :], axis=1))
        col_scale = target / list_mass(jnp.sum(kernel * row_scale[:, None], axis=0))
    row_scale = 1.0 / point_mass(jnp.sum(kernel * col_scale[None, :], axis=1))
    col_part = jnp.sum(kernel * row_scale[:, None], axis=0)

    weighted = scatter_rows(points).astype(jnp.float32) * row_scale[:, None]
    sums = lax.dot_general(
        weighted,
        kernel,
        (((0,), (0,)), ((), ())),
        precision=lax.Precision.HIGHEST,
        preferred_element_type=jnp.float32,
    )
    blocks = lax.axis_size(PTS)
    rows = sums.shape[0] // blocks
    packed = jnp.concatenate(
        [
            sums.reshape(blocks, rows, n_lists),
            jnp.broadcast_to(col_part[None, None, :], (blocks, 1, n_lists)),
        ],
        axis=1,
    ).reshape(blocks * (rows + 1), n_lists)
    reduced = sum_scatter(packed)
    col_total = reduced[rows]
    return (reduced[:rows] / col_total[None, :], jnp.log(target / col_total))


def solution(mesh):
    sizes = [size for _, size in PTS_AXES + LISTS_AXES]
    assert mesh.shape["pts"] == sizes[0] * sizes[1] * sizes[2]
    assert mesh.shape["lists"] == sizes[3] * sizes[4]
    fine = Mesh(mesh.devices.reshape(sizes), PTS + LISTS)
    return jax.shard_map(
        local,
        mesh=fine,
        in_specs=(P(PTS, None), P(LISTS, None), P(PTS), P(LISTS)),
        out_specs=(P(PTS, LISTS), P(LISTS)),
        check_vma=False,
    )
```

```python
import jax
import jax.numpy as jnp
from jax import lax
from jax.sharding import Mesh, PartitionSpec as P

ITERS = 3


def kernel_tile(points, cent_block, prior, start):
    score = lax.dot_general(
        points, cent_block, (((1,), (1,)), ((), ())), preferred_element_type=jnp.float32
    )
    cols = start + lax.iota(jnp.int32, cent_block.shape[0])
    hit = (prior[:, None] == cols[None, :]).astype(jnp.float32)
    return jnp.exp(3.0 * score + 10.0 * hit)


PTS_AXES = (("z_hi", 4), ("y", 4), ("core", 2))
LISTS_AXES = (("x", 4), ("z_lo", 4))
PTS = tuple(name for name, _ in PTS_AXES)
LISTS = tuple(name for name, _ in LISTS_AXES)


def exchange_sum(value, names):
    n = lax.axis_size(names)
    copies = jnp.broadcast_to(value[None], (n,) + value.shape)
    return jnp.sum(lax.all_to_all(copies, names, 0, 0), axis=0)


def point_mass(partial_value):
    return exchange_sum(partial_value, LISTS)


def list_mass(partial_value):
    return exchange_sum(exchange_sum(partial_value, ("y", "core")), "z_hi")


def scatter_rows(points):
    n = points.shape[0]
    sizes = [size for _, size in PTS_AXES]
    rows = points.shape[1] // (sizes[0] * sizes[1] * sizes[2])
    blocked = points.reshape(n, sizes[0], sizes[1], sizes[2], rows)
    return blocked.transpose(0, 3, 2, 1, 4).reshape(n, points.shape[1])


def sum_scatter(value):
    for name in ("core", "y", "z_hi"):
        n = lax.axis_size(name)
        blocks = value.reshape(n, value.shape[0] // n, value.shape[1])
        value = jnp.sum(lax.all_to_all(blocks, name, 0, 0), axis=0)
    return value


def local(points, centroids, prior, loads):
    n_lists = centroids.shape[0]
    offset = (lax.axis_index("x") * lax.axis_size("z_lo") + lax.axis_index("z_lo")) * n_lists
    total_pts = points.shape[0] * lax.axis_size(PTS)
    total_lists = n_lists * lax.axis_size(LISTS)
    target = loads.astype(jnp.float32) * (total_pts / (8.0 * total_lists))

    kernel = kernel_tile(points, centroids, prior, offset)

    col_scale = jnp.ones((n_lists,), jnp.float32)
    for step in range(ITERS - 1):
        row_scale = 1.0 / point_mass(jnp.sum(kernel * col_scale[None, :], axis=1))
        col_scale = target / list_mass(jnp.sum(kernel * row_scale[:, None], axis=0))
    row_scale = 1.0 / point_mass(jnp.sum(kernel * col_scale[None, :], axis=1))
    col_part = jnp.sum(kernel * row_scale[:, None], axis=0)

    weighted = scatter_rows(points).astype(jnp.float32) * row_scale[:, None]
    lanes = 512
    chunks = n_lists // lanes
    sums = lax.dot_general(
        weighted,
        kernel.reshape(kernel.shape[0], chunks, lanes),
        (((0,), (0,)), ((), ())),
        precision=lax.Precision.HIGH,
        preferred_element_type=jnp.float32,
    )
    blocks = lax.axis_size(PTS)
    rows = sums.shape[0] // blocks
    packed = jnp.concatenate(
        [
            sums.reshape(blocks, rows * chunks, lanes),
            jnp.broadcast_to(col_part.reshape(1, chunks, lanes), (blocks, chunks, lanes)),
        ],
        axis=1,
    ).reshape(blocks * (rows + 1) * chunks, lanes)
    reduced = sum_scatter(packed)
    col_total = reduced[rows * chunks :].reshape(n_lists)
    means = reduced[: rows * chunks].reshape(rows, n_lists) / col_total[None, :]
    return (means, jnp.log(target / col_total))


def solution(mesh):
    sizes = [size for _, size in PTS_AXES + LISTS_AXES]
    assert mesh.shape["pts"] == sizes[0] * sizes[1] * sizes[2]
    assert mesh.shape["lists"] == sizes[3] * sizes[4]
    fine = Mesh(mesh.devices.reshape(sizes), PTS + LISTS)
    return jax.shard_map(
        local,
        mesh=fine,
        in_specs=(P(PTS, None), P(LISTS, None), P(PTS), P(LISTS)),
        out_specs=(P(PTS, LISTS), P(LISTS)),
        check_vma=False,
    )
```

```python
import jax
import jax.numpy as jnp
from jax import lax
from jax.sharding import Mesh, PartitionSpec as P

ITERS = 3


def kernel_tile(points, cent_block, prior, start):
    score = lax.dot_general(
        points, cent_block, (((1,), (1,)), ((), ())), preferred_element_type=jnp.float32
    )
    cols = start + lax.iota(jnp.int32, cent_block.shape[0])
    hit = (prior[:, None] == cols[None, :]).astype(jnp.float32)
    return jnp.exp(3.0 * score + 10.0 * hit)


PTS_AXES = (("z_hi", 4), ("y", 4), ("core", 2))
LISTS_AXES = (("x", 4), ("z_lo", 4))
PTS = tuple(name for name, _ in PTS_AXES)
LISTS = tuple(name for name, _ in LISTS_AXES)


def exchange_sum(value, names):
    n = lax.axis_size(names)
    copies = jnp.broadcast_to(value[None], (n,) + value.shape)
    return jnp.sum(lax.all_to_all(copies, names, 0, 0), axis=0)


def point_mass(partial_value):
    return exchange_sum(partial_value, LISTS)


def list_mass(partial_value):
    return exchange_sum(exchange_sum(partial_value, ("y", "core")), "z_hi")


def scatter_rows(points):
    n = points.shape[0]
    sizes = [size for _, size in PTS_AXES]
    rows = points.shape[1] // (sizes[0] * sizes[1] * sizes[2])
    blocked = points.reshape(n, sizes[0], sizes[1], sizes[2], rows)
    return blocked.transpose(0, 3, 2, 1, 4).reshape(n, points.shape[1])


def sum_scatter(value):
    for name in ("core", "y", "z_hi"):
        n = lax.axis_size(name)
        blocks = value.reshape(n, value.shape[0] // n, value.shape[1])
        value = jnp.sum(lax.all_to_all(blocks, name, 0, 0), axis=0)
    return value


def local(points, centroids, prior, loads):
    n_lists = centroids.shape[0]
    offset = (lax.axis_index("x") * lax.axis_size("z_lo") + lax.axis_index("z_lo")) * n_lists
    total_pts = points.shape[0] * lax.axis_size(PTS)
    total_lists = n_lists * lax.axis_size(LISTS)
    target = loads.astype(jnp.float32) * (total_pts / (8.0 * total_lists))

    kernel = kernel_tile(points, centroids, prior, offset)

    col_scale = jnp.ones((n_lists,), jnp.float32)
    for step in range(ITERS - 1):
        row_scale = 1.0 / point_mass(jnp.sum(kernel * col_scale[None, :], axis=1))
        col_scale = target / list_mass(jnp.sum(kernel * row_scale[:, None], axis=0))
    row_scale = 1.0 / point_mass(jnp.sum(kernel * col_scale[None, :], axis=1))

    n_pts, dim = points.shape
    weighted = jnp.concatenate(
        [
            scatter_rows(points).astype(jnp.float32) * row_scale[:, None],
            row_scale[:, None],
            jnp.zeros((n_pts, 7), jnp.float32),
        ],
        axis=1,
    )
    lanes = 512
    chunks = n_lists // lanes
    product = lax.dot_general(
        weighted,
        kernel.reshape(n_pts, chunks, lanes),
        (((0,), (0,)), ((), ())),
        precision=lax.Precision.HIGH,
        preferred_element_type=jnp.float32,
    )
    sums = product[:dim]
    col_part = product[dim]
    blocks = lax.axis_size(PTS)
    rows = sums.shape[0] // blocks
    packed = jnp.concatenate(
        [
            sums.reshape(blocks, rows * chunks, lanes),
            jnp.broadcast_to(col_part[None], (blocks, chunks, lanes)),
        ],
        axis=1,
    ).reshape(blocks * (rows + 1) * chunks, lanes)
    reduced = sum_scatter(packed)
    col_total = reduced[rows * chunks :].reshape(n_lists)
    means = reduced[: rows * chunks].reshape(rows, n_lists) / col_total[None, :]
    return (means, jnp.log(target / col_total))


def solution(mesh):
    sizes = [size for _, size in PTS_AXES + LISTS_AXES]
    assert mesh.shape["pts"] == sizes[0] * sizes[1] * sizes[2]
    assert mesh.shape["lists"] == sizes[3] * sizes[4]
    fine = Mesh(mesh.devices.reshape(sizes), PTS + LISTS)
    return jax.shard_map(
        local,
        mesh=fine,
        in_specs=(P(PTS, None), P(LISTS, None), P(PTS), P(LISTS)),
        out_specs=(P(PTS, LISTS), P(LISTS)),
        check_vma=False,
    )
```

```python
import jax
import jax.numpy as jnp
from jax import lax
from jax.sharding import Mesh, PartitionSpec as P

ITERS = 3


def kernel_tile(points, cent_block, prior, start):
    score = lax.dot_general(
        points, cent_block, (((1,), (1,)), ((), ())), preferred_element_type=jnp.float32
    )
    cols = start + lax.iota(jnp.int32, cent_block.shape[0])
    hit = (prior[:, None] == cols[None, :]).astype(jnp.float32)
    return jnp.exp(3.0 * score + 10.0 * hit)


PTS_AXES = (("z_hi", 4), ("y", 4), ("core", 2))
LISTS_AXES = (("x", 4), ("z_lo", 4))
PTS = tuple(name for name, _ in PTS_AXES)
LISTS = tuple(name for name, _ in LISTS_AXES)


def exchange_sum(value, names):
    n = lax.axis_size(names)
    copies = jnp.broadcast_to(value[None], (n,) + value.shape)
    return jnp.sum(lax.all_to_all(copies, names, 0, 0), axis=0)


def point_mass(partial_value):
    return exchange_sum(partial_value, LISTS)


def list_mass(partial_value):
    return exchange_sum(exchange_sum(partial_value, ("y", "core")), "z_hi")


def scatter_rows(points):
    n = points.shape[0]
    sizes = [size for _, size in PTS_AXES]
    rows = points.shape[1] // (sizes[0] * sizes[1] * sizes[2])
    blocked = points.reshape(n, sizes[0], sizes[1], sizes[2], rows)
    return blocked.transpose(0, 3, 2, 1, 4).reshape(n, points.shape[1])


def exchange_scatter(value, name):
    n = lax.axis_size(name)
    blocks = value.reshape(n, value.shape[0] // n, value.shape[1])
    return jnp.sum(lax.all_to_all(blocks, name, 0, 0), axis=0)


def permute_scatter(value, name):
    n = lax.axis_size(name)
    me = lax.axis_index(name)
    blocks = value.reshape(n, value.shape[0] // n, value.shape[1])
    total = lax.dynamic_index_in_dim(blocks, me, 0, keepdims=False)
    for shift in range(1, n):
        outgoing = lax.dynamic_index_in_dim(blocks, (me + shift) % n, 0, keepdims=False)
        total = total + lax.ppermute(outgoing, name, [(i, (i + shift) % n) for i in range(n)])
    return total


def sum_scatter(value):
    value = exchange_scatter(value, "core")
    width = value.shape[1] // 2
    first = permute_scatter(value[:, :width], "y")
    first, rest = lax.optimization_barrier((first, value[:, width:]))
    second = permute_scatter(rest, "y")
    first = permute_scatter(first, "z_hi")
    second = permute_scatter(second, "z_hi")
    return jnp.concatenate([first, second], axis=1)


def local(points, centroids, prior, loads):
    n_lists = centroids.shape[0]
    offset = (lax.axis_index("x") * lax.axis_size("z_lo") + lax.axis_index("z_lo")) * n_lists
    total_pts = points.shape[0] * lax.axis_size(PTS)
    total_lists = n_lists * lax.axis_size(LISTS)
    target = loads.astype(jnp.float32) * (total_pts / (8.0 * total_lists))

    kernel = kernel_tile(points, centroids, prior, offset)

    col_scale = jnp.ones((n_lists,), jnp.float32)
    for step in range(ITERS - 1):
        row_scale = 1.0 / point_mass(jnp.sum(kernel * col_scale[None, :], axis=1))
        col_scale = target / list_mass(jnp.sum(kernel * row_scale[:, None], axis=0))
    row_scale = 1.0 / point_mass(jnp.sum(kernel * col_scale[None, :], axis=1))

    n_pts, dim = points.shape
    weighted = jnp.concatenate(
        [
            scatter_rows(points).astype(jnp.float32) * row_scale[:, None],
            row_scale[:, None],
            jnp.zeros((n_pts, 7), jnp.float32),
        ],
        axis=1,
    )
    lanes = 512
    chunks = n_lists // lanes
    product = lax.dot_general(
        weighted,
        kernel.reshape(n_pts, chunks, lanes),
        (((0,), (0,)), ((), ())),
        precision=lax.Precision.HIGH,
        preferred_element_type=jnp.float32,
    )
    sums = product[:dim]
    col_part = product[dim]
    blocks = lax.axis_size(PTS)
    rows = sums.shape[0] // blocks
    packed = jnp.concatenate(
        [
            sums.reshape(blocks, rows * chunks, lanes),
            jnp.broadcast_to(col_part[None], (blocks, chunks, lanes)),
        ],
        axis=1,
    ).reshape(blocks * (rows + 1) * chunks, lanes)
    reduced = sum_scatter(packed)
    col_total = reduced[rows * chunks :].reshape(n_lists)
    means = reduced[: rows * chunks].reshape(rows, n_lists) / col_total[None, :]
    return (means, jnp.log(target / col_total))


def solution(mesh):
    sizes = [size for _, size in PTS_AXES + LISTS_AXES]
    assert mesh.shape["pts"] == sizes[0] * sizes[1] * sizes[2]
    assert mesh.shape["lists"] == sizes[3] * sizes[4]
    fine = Mesh(mesh.devices.reshape(sizes), PTS + LISTS)
    return jax.shard_map(
        local,
        mesh=fine,
        in_specs=(P(PTS, None), P(LISTS, None), P(PTS), P(LISTS)),
        out_specs=(P(PTS, LISTS), P(LISTS)),
        check_vma=False,
    )
```

```python
import jax
import jax.numpy as jnp
from jax import lax
from jax.sharding import Mesh, PartitionSpec as P

ITERS = 3


def kernel_tile(points, cent_block, prior, start):
    score = lax.dot_general(
        points, cent_block, (((1,), (1,)), ((), ())), preferred_element_type=jnp.float32
    )
    cols = start + lax.iota(jnp.int32, cent_block.shape[0])
    hit = (prior[:, None] == cols[None, :]).astype(jnp.float32)
    return jnp.exp(3.0 * score + 10.0 * hit)


PTS_AXES = (("z_hi", 4), ("y", 4), ("core", 2))
LISTS_AXES = (("x", 4), ("z_lo", 4))
PTS = tuple(name for name, _ in PTS_AXES)
LISTS = tuple(name for name, _ in LISTS_AXES)


def exchange_sum(value, names):
    n = lax.axis_size(names)
    copies = jnp.broadcast_to(value[None], (n,) + value.shape)
    return jnp.sum(lax.all_to_all(copies, names, 0, 0), axis=0)


def point_mass(partial_value):
    return exchange_sum(partial_value, LISTS)


def list_mass(partial_value):
    return exchange_sum(exchange_sum(partial_value, ("y", "core")), "z_hi")


def scatter_rows(points):
    n = points.shape[0]
    sizes = [size for _, size in PTS_AXES]
    rows = points.shape[1] // (sizes[0] * sizes[1] * sizes[2])
    blocked = points.reshape(n, sizes[0], sizes[1], sizes[2], rows)
    return blocked.transpose(0, 3, 2, 1, 4).reshape(n, points.shape[1])


def sum_scatter(value):
    for name in ("core", "y", "z_hi"):
        n = lax.axis_size(name)
        blocks = value.reshape(n, value.shape[0] // n, value.shape[1])
        value = jnp.sum(lax.all_to_all(blocks, name, 0, 0), axis=0)
    return value


def local(points, centroids, prior, loads):
    n_lists = centroids.shape[0]
    offset = (lax.axis_index("x") * lax.axis_size("z_lo") + lax.axis_index("z_lo")) * n_lists
    total_pts = points.shape[0] * lax.axis_size(PTS)
    total_lists = n_lists * lax.axis_size(LISTS)
    target = loads.astype(jnp.float32) * (total_pts / (8.0 * total_lists))

    kernel = kernel_tile(points, centroids, prior, offset)

    col_scale = jnp.ones((n_lists,), jnp.float32)
    for step in range(ITERS - 1):
        row_scale = 1.0 / point_mass(jnp.sum(kernel * col_scale[None, :], axis=1))
        col_scale = target / list_mass(jnp.sum(kernel * row_scale[:, None], axis=0))
    row_scale = 1.0 / point_mass(jnp.sum(kernel * col_scale[None, :], axis=1))

    n_pts, dim = points.shape
    weighted = jnp.concatenate(
        [scatter_rows(points), jnp.ones((n_pts, 1), points.dtype), jnp.zeros((n_pts, 7), points.dtype)],
        axis=1,
    )
    scaled = kernel * row_scale[:, None]
    high = scaled.astype(jnp.bfloat16)
    low = (scaled - high.astype(jnp.float32)).astype(jnp.bfloat16)
    lanes = 512
    chunks = n_lists // lanes

    def times(part):
        return lax.dot_general(
            weighted,
            part.reshape(n_pts, chunks, lanes),
            (((0,), (0,)), ((), ())),
            preferred_element_type=jnp.float32,
        )

    product = times(high) + times(low)
    sums = product[:dim]
    col_part = product[dim]
    blocks = lax.axis_size(PTS)
    rows = sums.shape[0] // blocks
    packed = jnp.concatenate(
        [
            sums.reshape(blocks, rows * chunks, lanes),
            jnp.broadcast_to(col_part[None], (blocks, chunks, lanes)),
        ],
        axis=1,
    ).reshape(blocks * (rows + 1) * chunks, lanes)
    reduced = sum_scatter(packed)
    col_total = reduced[rows * chunks :].reshape(n_lists)
    means = reduced[: rows * chunks].reshape(rows, n_lists) / col_total[None, :]
    return (means, jnp.log(target / col_total))


def solution(mesh):
    sizes = [size for _, size in PTS_AXES + LISTS_AXES]
    assert mesh.shape["pts"] == sizes[0] * sizes[1] * sizes[2]
    assert mesh.shape["lists"] == sizes[3] * sizes[4]
    fine = Mesh(mesh.devices.reshape(sizes), PTS + LISTS)
    return jax.shard_map(
        local,
        mesh=fine,
        in_specs=(P(PTS, None), P(LISTS, None), P(PTS), P(LISTS)),
        out_specs=(P(PTS, LISTS), P(LISTS)),
        check_vma=False,
    )
```

```python
import jax
import jax.numpy as jnp
from jax import lax
from jax.sharding import Mesh, PartitionSpec as P

ITERS = 3


def kernel_tile(points, cent_block, prior, start):
    score = lax.dot_general(
        points, cent_block, (((1,), (1,)), ((), ())), preferred_element_type=jnp.float32
    )
    cols = start + lax.iota(jnp.int32, cent_block.shape[0])
    hit = (prior[:, None] == cols[None, :]).astype(jnp.float32)
    return jnp.exp(3.0 * score + 10.0 * hit)


PTS_AXES = (("z_hi", 4), ("y", 4), ("core", 2))
LISTS_AXES = (("x", 4), ("z_lo", 4))
PTS = tuple(name for name, _ in PTS_AXES)
LISTS = tuple(name for name, _ in LISTS_AXES)


def exchange_sum(value, names):
    n = lax.axis_size(names)
    copies = jnp.broadcast_to(value[None], (n,) + value.shape)
    return jnp.sum(lax.all_to_all(copies, names, 0, 0), axis=0)


def point_mass(partial_value):
    return exchange_sum(partial_value, LISTS)


def list_mass(partial_value):
    return exchange_sum(exchange_sum(partial_value, ("y", "core")), "z_hi")


def scatter_rows(points):
    n = points.shape[0]
    sizes = [size for _, size in PTS_AXES]
    rows = points.shape[1] // (sizes[0] * sizes[1] * sizes[2])
    blocked = points.reshape(n, sizes[0], sizes[1], sizes[2], rows)
    return blocked.transpose(0, 3, 2, 1, 4).reshape(n, points.shape[1])


def sum_scatter(value):
    for name in ("core", "y", "z_hi"):
        n = lax.axis_size(name)
        blocks = value.reshape(n, value.shape[0] // n, value.shape[1])
        value = jnp.sum(lax.all_to_all(blocks, name, 0, 0), axis=0)
    return value


def local(points, centroids, prior, loads):
    n_lists = centroids.shape[0]
    offset = (lax.axis_index("x") * lax.axis_size("z_lo") + lax.axis_index("z_lo")) * n_lists
    total_pts = points.shape[0] * lax.axis_size(PTS)
    total_lists = n_lists * lax.axis_size(LISTS)
    target = loads.astype(jnp.float32) * (total_pts / (8.0 * total_lists))

    pieces = 2
    width = n_lists // pieces
    kernel = [
        kernel_tile(points, centroids[part * width : (part + 1) * width], prior, offset + part * width)
        for part in range(pieces)
    ]
    lanes = 512
    chunks = n_lists // lanes

    def row_totals(col_scale):
        return sum(
            jnp.sum(block * col_scale[None, part * width : (part + 1) * width], axis=1)
            for part, block in enumerate(kernel)
        )

    def col_totals(row_scale):
        return jnp.concatenate([jnp.sum(block * row_scale[:, None], axis=0) for block in kernel])

    col_scale = jnp.ones((n_lists,), jnp.float32)
    for step in range(ITERS - 1):
        row_scale = 1.0 / point_mass(row_totals(col_scale))
        col_scale = target / list_mass(col_totals(row_scale))
    row_scale = 1.0 / point_mass(row_totals(col_scale))

    n_pts, dim = points.shape
    weighted = jnp.concatenate(
        [
            scatter_rows(points).astype(jnp.float32) * row_scale[:, None],
            row_scale[:, None],
            jnp.zeros((n_pts, 7), jnp.float32),
        ],
        axis=1,
    )
    product = jnp.concatenate(
        [
            lax.dot_general(
                weighted,
                block.reshape(n_pts, width // lanes, lanes),
                (((0,), (0,)), ((), ())),
                precision=lax.Precision.HIGH,
                preferred_element_type=jnp.float32,
            )
            for block in kernel
        ],
        axis=1,
    )
    sums = product[:dim]
    col_part = product[dim]
    blocks = lax.axis_size(PTS)
    rows = sums.shape[0] // blocks
    packed = jnp.concatenate(
        [
            sums.reshape(blocks, rows * chunks, lanes),
            jnp.broadcast_to(col_part[None], (blocks, chunks, lanes)),
        ],
        axis=1,
    ).reshape(blocks * (rows + 1) * chunks, lanes)
    reduced = sum_scatter(packed)
    col_total = reduced[rows * chunks :].reshape(n_lists)
    means = reduced[: rows * chunks].reshape(rows, n_lists) / col_total[None, :]
    return (means, jnp.log(target / col_total))


def solution(mesh):
    sizes = [size for _, size in PTS_AXES + LISTS_AXES]
    assert mesh.shape["pts"] == sizes[0] * sizes[1] * sizes[2]
    assert mesh.shape["lists"] == sizes[3] * sizes[4]
    fine = Mesh(mesh.devices.reshape(sizes), PTS + LISTS)
    return jax.shard_map(
        local,
        mesh=fine,
        in_specs=(P(PTS, None), P(LISTS, None), P(PTS), P(LISTS)),
        out_specs=(P(PTS, LISTS), P(LISTS)),
        check_vma=False,
    )
```

```python
import jax
import jax.numpy as jnp
from jax import lax
from jax.sharding import Mesh, PartitionSpec as P

ITERS = 3


def kernel_tile(points, cent_block, prior, start):
    score = lax.dot_general(
        points, cent_block, (((1,), (1,)), ((), ())), preferred_element_type=jnp.float32
    )
    cols = start + lax.iota(jnp.int32, cent_block.shape[0])
    hit = (prior[:, None] == cols[None, :]).astype(jnp.float32)
    return jnp.exp(3.0 * score + 10.0 * hit)


PTS_AXES = (("z_hi", 4), ("y", 4), ("core", 2))
LISTS_AXES = (("x", 4), ("z_lo", 4))
PTS = tuple(name for name, _ in PTS_AXES)
LISTS = tuple(name for name, _ in LISTS_AXES)


def exchange_sum(value, names):
    n = lax.axis_size(names)
    copies = jnp.broadcast_to(value[None], (n,) + value.shape)
    return jnp.sum(lax.all_to_all(copies, names, 0, 0), axis=0)


def point_mass(partial_value):
    return exchange_sum(partial_value, LISTS)


def list_mass(partial_value):
    return exchange_sum(exchange_sum(partial_value, ("y", "core")), "z_hi")


def scatter_rows(points):
    n = points.shape[0]
    sizes = [size for _, size in PTS_AXES]
    rows = points.shape[1] // (sizes[0] * sizes[1] * sizes[2])
    blocked = points.reshape(n, sizes[0], sizes[1], sizes[2], rows)
    return blocked.transpose(0, 3, 2, 1, 4).reshape(n, points.shape[1])


def sum_scatter(value):
    for name in ("core", "y", "z_hi"):
        n = lax.axis_size(name)
        blocks = value.reshape(n, value.shape[0] // n, value.shape[1])
        value = jnp.sum(lax.all_to_all(blocks, name, 0, 0), axis=0)
    return value


def local(points, centroids, prior, loads):
    n_lists = centroids.shape[0]
    offset = (lax.axis_index("x") * lax.axis_size("z_lo") + lax.axis_index("z_lo")) * n_lists
    total_pts = points.shape[0] * lax.axis_size(PTS)
    total_lists = n_lists * lax.axis_size(LISTS)
    target = loads.astype(jnp.float32) * (total_pts / (8.0 * total_lists))

    pieces = 2
    width = n_lists // pieces
    kernel = [
        kernel_tile(points, centroids[part * width : (part + 1) * width], prior, offset + part * width)
        for part in range(pieces)
    ]
    lanes = 512
    chunks = n_lists // lanes

    def row_totals(col_scale):
        return sum(
            jnp.sum(block * col_scale[None, part * width : (part + 1) * width], axis=1)
            for part, block in enumerate(kernel)
        )

    def col_totals(row_scale):
        return jnp.concatenate([jnp.sum(block * row_scale[:, None], axis=0) for block in kernel])

    col_scale = jnp.ones((n_lists,), jnp.float32)
    for step in range(ITERS - 1):
        row_scale = 1.0 / point_mass(row_totals(col_scale))
        col_scale = target / list_mass(col_totals(row_scale))
    last_rows = row_totals(col_scale)
    high = lax.optimization_barrier([block.astype(jnp.bfloat16) for block in kernel])
    low = [(block - part.astype(jnp.float32)).astype(jnp.bfloat16) for block, part in zip(kernel, high)]
    row_scale = 1.0 / point_mass(last_rows)

    n_pts, dim = points.shape
    weighted = jnp.concatenate(
        [
            scatter_rows(points).astype(jnp.float32) * row_scale[:, None],
            row_scale[:, None],
            jnp.zeros((n_pts, 7), jnp.float32),
        ],
        axis=1,
    )
    weighted_high = lax.optimization_barrier(weighted.astype(jnp.bfloat16))
    weighted_low = (weighted - weighted_high.astype(jnp.float32)).astype(jnp.bfloat16)

    def times(left, right):
        return lax.dot_general(
            left,
            right.reshape(n_pts, right.shape[1] // lanes, lanes),
            (((0,), (0,)), ((), ())),
            preferred_element_type=jnp.float32,
        )

    product = jnp.concatenate(
        [
            times(weighted_high, big) + times(weighted_high, small) + times(weighted_low, big)
            for big, small in zip(high, low)
        ],
        axis=1,
    )
    sums = product[:dim]
    col_part = product[dim]
    blocks = lax.axis_size(PTS)
    rows = sums.shape[0] // blocks
    packed = jnp.concatenate(
        [
            sums.reshape(blocks, rows * chunks, lanes),
            jnp.broadcast_to(col_part[None], (blocks, chunks, lanes)),
        ],
        axis=1,
    ).reshape(blocks * (rows + 1) * chunks, lanes)
    reduced = sum_scatter(packed)
    col_total = reduced[rows * chunks :].reshape(n_lists)
    means = reduced[: rows * chunks].reshape(rows, n_lists) / col_total[None, :]
    return (means, jnp.log(target / col_total))


def solution(mesh):
    sizes = [size for _, size in PTS_AXES + LISTS_AXES]
    assert mesh.shape["pts"] == sizes[0] * sizes[1] * sizes[2]
    assert mesh.shape["lists"] == sizes[3] * sizes[4]
    fine = Mesh(mesh.devices.reshape(sizes), PTS + LISTS)
    return jax.shard_map(
        local,
        mesh=fine,
        in_specs=(P(PTS, None), P(LISTS, None), P(PTS), P(LISTS)),
        out_specs=(P(PTS, LISTS), P(LISTS)),
        check_vma=False,
    )
```
